768 devices in a mesh: dp: 16 (over x_hi, y), blk: 48 (over z, x_lo, core).
Axes of the slice: x: 4 (x_hi: 2, x_lo: 2; x = x_hi * 2 + x_lo), y: 8, z: 12, core: 2. Of those that a mesh axis runs over, the one named last changes fastest.
Arguments:
- tokens: bfloat16 [16, 48, 128, 4096], P('dp', 'blk'), may hold values from -6 to 6
- cotangent: bfloat16 [16, 48, 128, 4096], P('dp', 'blk'), may hold values from -6 to 6
- gate_weight: bfloat16 [4096, 14784], P(None, 'blk'), may hold values from -0.09375 to 0.09375
- up_weight: bfloat16 [4096, 14784], P(None, 'blk'), may hold values from -0.09375 to 0.09375
- down_weight: bfloat16 [4096, 14784], P(None, 'blk'), may hold values from -0.046875 to 0.046875
- counts: int32 [16, 48], P('dp', 'blk'), may hold values from 64 to 128, as said below
- seg_ids: int32 [16, 48, 128], P('dp', 'blk'), may hold values from 0 to 3, never falling along the last dimension, each value on 1 to 64 neighbouring positions
- pair_side: int32 [16, 48, 4], P('dp', 'blk'), may hold values 0 or 1
Outputs:
- grad_tokens: bfloat16 [16, 48, 128, 4096], P('dp', 'blk')
- panel_grads: float32 [3, 4096, 14784], P(None, 'dp', 'blk')
The draws below stay inside these ranges and needn't reach their ends.
Inputs may be any that keep to these rules, and one draw needn't show every extreme that they name: `counts`: each device's count lies between 64 and 128; in every draw some device's count is exactly 128.
All inputs are finite; a program needn't handle non-finite values. No bound on the sum of `pair_side` on one device may be relied on, other than what follows from the above.
Results may differ from the reference program's by a relative error of at most 0.017.
Values may be sent and summed in bfloat16 or wider, within the bound.
No kernel may reach another device: no remote copies, remote signals or barrier semaphores. Data moves between devices by JAX's collectives and lax.ppermute only.
A program may use at most 64 MiB of HBM per device.

```python
import math
import jax
import jax.numpy as jnp
import numpy as np
from jax import lax

D = 4096
FF_DEV = 308
CAP = 128
SEQS = 4
FF = 14784
N_DP = 16
N_BLK = 48


def draw_counts(key, part):
    key_levels, key_full = jax.random.split(key)
    levels = jax.random.randint(key_levels, (N_DP * N_BLK,), CAP // 2, CAP + 1)
    chosen_slot = jax.random.randint(key_full, (), 0, N_DP * N_BLK)
    levels = jnp.where(jnp.arange(N_DP * N_BLK) == chosen_slot, CAP, levels)
    return levels.reshape(N_DP, N_BLK).astype(jnp.int32)


def set_ends(values, stream_key, low, high):
    longest = values.shape.index(max(values.shape))
    spots = []
    for shift in (0, 1):
        where = [jax.random.randint(jax.random.fold_in(stream_key, axis), (), 0, length) for axis, length in enumerate(values.shape)]
        where[longest] = (where[longest] + shift) % values.shape[longest]
        spots.append(tuple(where))
    return values.at[spots[0]].set(low).at[spots[1]].set(high)


def with_spikes(values, key, source, target, blocks, factor):
    def block_of(axis_at):
        return (jnp.arange(values.shape[axis_at]) // (values.shape[axis_at] // blocks)).reshape((-1,) + (1,) * (values.ndim - 1 - axis_at))

    first = jax.random.permutation(key, blocks)[block_of(target)]
    far = (block_of(target) + blocks // 2) % blocks
    return jnp.where((block_of(source) == first) | (block_of(source) == far), factor * values, values)


def steps_of(own_key, extent, shards, smallest, high):
    loudness = 1.0
    for axis_at, blocks in shards:
        steps = jax.random.uniform(jax.random.fold_in(jax.random.fold_in(own_key, 6), axis_at), (blocks,), jnp.float32, smallest / len(shards), high / len(shards))
        loudness = loudness * jnp.repeat(jnp.exp(steps), extent[axis_at] // blocks).reshape((-1,) + (1,) * (len(extent) - 1 - axis_at))
    return loudness


def split_up(number_of, total, most, skew):
    weights = [(1 << 20) // math.isqrt(grade ** skew) + 1 for grade in range(2, number_of + 1)]
    rest, given = total - most - (number_of - 1), [1] * (number_of - 1)
    while rest > 0:
        candidates = [i for i in range(number_of - 1) if given[i] < most]
        whole, budget = sum([weights[i] for i in candidates]), rest
        for i in candidates:
            more = min(most - given[i], max(1, budget * weights[i] // whole), rest)
            given[i] = given[i] + more
            rest = rest - more
    return np.array([most] + given)


def ragged(rng, count, total, most, skew):
    if count == 2:
        one = jax.random.randint(rng, (), max(1, total - most), min(most, total - 1) + 1)
        return jnp.stack([one, total - one])
    lengths = jnp.asarray(split_up(count, total, most, skew), jnp.int32)
    pairs = (count - 1) // 2
    donor, sink = lengths[1:1 + 2 * pairs:2], lengths[2:2 + 2 * pairs:2]
    room = jnp.minimum(donor - 1, most - sink)
    shifted = jax.random.randint(jax.random.fold_in(rng, 1), (pairs,), 0, 1 << 20) % (room + 1)
    lengths = lengths.at[1:1 + 2 * pairs:2].set(donor - shifted).at[2:2 + 2 * pairs:2].set(sink + shifted)
    return lengths[jax.random.permutation(jax.random.fold_in(rng, 2), count)]


def noise(own_key, extent, deviation, limit, pieces=(), held_as=jnp.bfloat16):
    entries = deviation * jax.random.normal(own_key, extent, jnp.float32)
    if pieces:
        entries = entries * steps_of(own_key, extent, pieces, -0.22, 0.18)
    return jnp.clip(entries, -limit, limit).astype(held_as)


def noise_with(rng, shape, spread, limit, pieces, heavy, kind=jnp.bfloat16):
    result = spread * jax.random.normal(rng, shape, jnp.float32)
    if pieces:
        result = result * steps_of(rng, shape, pieces, -0.22, 0.18)
    return jnp.clip(with_spikes(result, jax.random.fold_in(rng, 3), *heavy), -limit, limit).astype(kind)


def setup_inputs(seed: int = 0) -> dict:
    seeds = jax.random.split(jax.random.key(seed), 9)
    return {
        "tokens": noise_with(seeds[0], (N_DP, N_BLK, CAP, D), 1.0, 6.0, ((0, 16), (1, 48)), (0, 3, 16, 2.0)),
        "cotangent": noise(seeds[1], (N_DP, N_BLK, CAP, D), 1.0, 6.0, ((0, 16), (1, 48))),
        "gate_weight": noise(seeds[2], (D, FF), D ** -0.5, 0.09375, ((1, 48),)),
        "up_weight": noise(seeds[3], (D, FF), D ** -0.5, 0.09375, ((1, 48),)),
        "down_weight": noise(seeds[4], (D, FF), FF ** -0.5, 0.046875, ((1, 48),)),
        "counts": draw_counts(jax.random.fold_in(seeds[8], 71), 0),
        "seg_ids": jax.vmap(lambda own: jnp.searchsorted(jnp.cumsum(ragged(own, SEQS, CAP, CAP // 2, 0)), jnp.arange(CAP), side="right"))(jax.random.split(seeds[6], N_DP * N_BLK)).reshape((N_DP, N_BLK, CAP)).astype(jnp.int32),
        "pair_side": set_ends((jax.random.randint(seeds[7], (N_DP, N_BLK, SEQS), 0, 2) < 1).astype(jnp.int32), jax.random.fold_in(seeds[7], 1), 0, 1),
    }


def token_weights(counts, seg_ids, pair_side):
    positions = jnp.arange(seg_ids.shape[-1], dtype=jnp.int32)
    valid_rows = positions[None, None, :] < counts[:, :, None]
    member = (seg_ids[..., None] == jnp.arange(SEQS, dtype=jnp.int32)) & valid_rows[..., None]
    member_f = member.astype(jnp.float32)
    length = jnp.sum(member_f, axis=2)
    half_span = jnp.float32(CAP) / jnp.float32(SEQS)
    seq_weight = (2.0 * pair_side.astype(jnp.float32) - 1.0) * half_span / (length + half_span)
    return jnp.sum(member_f * seq_weight[:, :, None, :], axis=3)


def next_panels(weight):
    panel_split = weight.astype(jnp.float32).reshape(D, N_BLK, FF_DEV)
    return jnp.roll(jnp.transpose(panel_split, (1, 0, 2)), -1, axis=0)


def reference(tokens, cotangent, gate_weight, up_weight, down_weight, counts, seg_ids, pair_side):
    weights = token_weights(counts, seg_ids, pair_side)
    upstream = (cotangent.astype(jnp.float32) * weights[..., None]).astype(jnp.bfloat16)
    gate_panels = next_panels(gate_weight)
    up_panels = next_panels(up_weight)
    down_panels = next_panels(down_weight)
    high = lax.Precision.HIGHEST

    def one_group(running, inputs):
        tok_rows, grad_rows = inputs
        tok_f = tok_rows.astype(jnp.float32)
        grad_f = grad_rows.astype(jnp.float32)
        gate_pre = jnp.einsum('btd,bdp->btp', tok_f, gate_panels, precision=high)
        up_pre = jnp.einsum('btd,bdp->btp', tok_f, up_panels, precision=high)
        sigmoid_gate = jax.nn.sigmoid(gate_pre)
        gate_act = gate_pre * sigmoid_gate
        hidden = (gate_act * up_pre).astype(jnp.bfloat16)
        d_hidden = jnp.einsum('btd,bdp->btp', grad_f, down_panels, precision=high)
        d_gate = (d_hidden * up_pre * sigmoid_gate * (1.0 + gate_pre * (1.0 - sigmoid_gate))).astype(jnp.bfloat16)
        d_up = (d_hidden * gate_act).astype(jnp.bfloat16)
        grad_tok = jnp.einsum('btp,bdp->btd', d_gate.astype(jnp.float32), gate_panels, precision=high)
        grad_tok = grad_tok + jnp.einsum('btp,bdp->btd', d_up.astype(jnp.float32), up_panels, precision=high)
        grad_gate = jnp.einsum('btd,btp->bdp', tok_f, d_gate.astype(jnp.float32), precision=high)
        grad_up = jnp.einsum('btd,btp->bdp', tok_f, d_up.astype(jnp.float32), precision=high)
        grad_down = jnp.einsum('btd,btp->bdp', grad_f, hidden.astype(jnp.float32), precision=high)
        partial_sums = jnp.stack([grad_gate, grad_up, grad_down]).astype(jnp.bfloat16)
        partial_sums = lax.optimization_barrier(partial_sums)
        return running + partial_sums.astype(jnp.float32), grad_tok.astype(jnp.bfloat16)

    start = jnp.zeros((3, N_BLK, D, FF_DEV), jnp.float32)
    running, grad_tokens = lax.scan(one_group, start, (tokens, upstream))
    ordered = jnp.roll(running / N_DP, 1, axis=1)
    panel_grads = jnp.transpose(ordered, (0, 2, 1, 3)).reshape(3, D, N_BLK * FF_DEV)
    return grad_tokens, panel_grads
```

```python
import jax
import jax.numpy as jnp
from jax import lax
from jax.sharding import PartitionSpec as P

CAP = 128
SEQS = 4


def shifted(block, axis, distance):
    devices = range(lax.axis_size(axis))
    route = [((i - distance) % len(devices), i) for i in devices]
    return lax.ppermute(block, axis, route)


def token_weights(counts, seg_ids, pair_side):
    positions = jnp.arange(seg_ids.shape[-1], dtype=jnp.int32)
    valid_rows = positions[None, None, :] < counts[:, :, None]
    member = (seg_ids[..., None] == jnp.arange(SEQS, dtype=jnp.int32)) & valid_rows[..., None]
    member_f = member.astype(jnp.float32)
    length = jnp.sum(member_f, axis=2)
    half_span = jnp.float32(CAP) / jnp.float32(SEQS)
    seq_weight = (2.0 * pair_side.astype(jnp.float32) - 1.0) * half_span / (length + half_span)
    return jnp.sum(member_f * seq_weight[:, :, None, :], axis=3)


def contract_rows(left, right):
    return lax.dot_general(
        left, right, (((0,), (0,)), ((), ())), preferred_element_type=jnp.float32
    )


def contract_cols(left, right):
    return lax.dot_general(
        left, right, (((1,), (1,)), ((), ())), preferred_element_type=jnp.float32
    )


def backward_core(tok_rows, grad_rows, w_gate, w_up, w_down):
    gate_pre = jnp.dot(tok_rows, w_gate, preferred_element_type=jnp.float32)
    up_pre = jnp.dot(tok_rows, w_up, preferred_element_type=jnp.float32)
    sigmoid_gate = jax.nn.sigmoid(gate_pre)
    gate_act = gate_pre * sigmoid_gate
    hidden = (gate_act * up_pre).astype(jnp.bfloat16)
    d_hidden = jnp.dot(grad_rows, w_down, preferred_element_type=jnp.float32)
    d_gate = (d_hidden * up_pre * sigmoid_gate * (1.0 + gate_pre * (1.0 - sigmoid_gate))).astype(
        jnp.bfloat16
    )
    d_up = (d_hidden * gate_act).astype(jnp.bfloat16)
    grad_tok = (contract_cols(d_gate, w_gate) + contract_cols(d_up, w_up)).astype(jnp.bfloat16)
    grad_gate = contract_rows(tok_rows, d_gate)
    grad_up = contract_rows(tok_rows, d_up)
    grad_down = contract_rows(grad_rows, hidden)
    summed = reduce_over_dp(jnp.stack([grad_gate, grad_up, grad_down]))
    return (grad_tok, summed / lax.axis_size("dp"))


def reduce_over_dp(parts):
    n = lax.axis_size("dp")
    nx = 2
    ny = n // nx
    index = lax.axis_index("dp")
    xh = index // ny
    y = index % ny
    three, width, cols = parts.shape
    half = width // n // 2
    view = parts.reshape(three, nx, ny, 2, half, cols)

    def chunk(c, h):
        return lax.dynamic_index_in_dim(view[:, :, :, h], c, axis=2, keepdims=False)

    fwd = [(a * ny + b, a * ny + (b + 1) % ny) for a in range(nx) for b in range(ny)]
    bwd = [(a * ny + b, a * ny + (b - 1) % ny) for a in range(nx) for b in range(ny)]
    acc_f = chunk((y + ny - 1) % ny, 0)
    acc_b = chunk((y + 1) % ny, 1)
    for s in range(ny - 1):
        recv_f = lax.ppermute(acc_f.astype(jnp.bfloat16), "dp", fwd)
        recv_b = lax.ppermute(acc_b.astype(jnp.bfloat16), "dp", bwd)
        acc_f = recv_f.astype(jnp.float32) + chunk((y + 2 * ny - 2 - s) % ny, 0)
        acc_b = recv_b.astype(jnp.float32) + chunk((y + 2 + s) % ny, 1)
    acc = jnp.stack([acc_f, acc_b], axis=2)
    mine = lax.dynamic_index_in_dim(acc, xh, axis=1, keepdims=False)
    other = lax.dynamic_index_in_dim(acc, 1 - xh, axis=1, keepdims=False)
    across = [(a * ny + b, (1 - a) * ny + b) for a in range(nx) for b in range(ny)]
    got = lax.ppermute(other.astype(jnp.bfloat16), "dp", across)
    return (mine + got.astype(jnp.float32)).reshape(three, 2 * half, cols)


def shards(tokens, cotangent, gate_weight, up_weight, down_weight, counts, seg_ids, pair_side):
    weights = token_weights(counts, seg_ids, pair_side)
    upstream = (cotangent.astype(jnp.float32) * weights[..., None]).astype(jnp.bfloat16)
    width = tokens.shape[-1]
    tok_rows = tokens.reshape(-1, width)
    grad_rows = upstream.reshape(-1, width)
    moved_rows, moved_grads = shifted((tok_rows, grad_rows), "blk", 1)
    grad_moved, panel_grads = backward_core(
        moved_rows, moved_grads, gate_weight, up_weight, down_weight
    )
    grad_tok = shifted(grad_moved, "blk", -1)
    return (grad_tok.reshape(tokens.shape), panel_grads)


def solution(mesh):
    placed = (
        P("dp", "blk", None, None),
        P("dp", "blk", None, None),
        P(None, "blk"),
        P(None, "blk"),
        P(None, "blk"),
        P("dp", "blk"),
        P("dp", "blk", None),
        P("dp", "blk", None),
    )
    return jax.shard_map(
        shards,
        mesh=mesh,
        in_specs=placed,
        out_specs=(P("dp", "blk", None, None), P(None, "dp", "blk")),
        check_vma=False,
    )
```

```python
import jax
import jax.numpy as jnp
from jax import lax
from jax.sharding import PartitionSpec as P

CAP = 128
SEQS = 4


def shifted(block, axis, distance):
    devices = range(lax.axis_size(axis))
    route = [((i - distance) % len(devices), i) for i in devices]
    return lax.ppermute(block, axis, route)


def token_weights(counts, seg_ids, pair_side):
    positions = jnp.arange(seg_ids.shape[-1], dtype=jnp.int32)
    valid_rows = positions[None, None, :] < counts[:, :, None]
    member = (seg_ids[..., None] == jnp.arange(SEQS, dtype=jnp.int32)) & valid_rows[..., None]
    member_f = member.astype(jnp.float32)
    length = jnp.sum(member_f, axis=2)
    half_span = jnp.float32(CAP) / jnp.float32(SEQS)
    seq_weight = (2.0 * pair_side.astype(jnp.float32) - 1.0) * half_span / (length + half_span)
    return jnp.sum(member_f * seq_weight[:, :, None, :], axis=3)


def contract_rows(left, right):
    return lax.dot_general(
        left, right, (((0,), (0,)), ((), ())), preferred_element_type=jnp.float32
    )


def contract_cols(left, right):
    return lax.dot_general(
        left, right, (((1,), (1,)), ((), ())), preferred_element_type=jnp.float32
    )


def backward_core(tok_rows, grad_rows, w_gate, w_up, w_down):
    gate_pre = jnp.dot(tok_rows, w_gate, preferred_element_type=jnp.float32)
    up_pre = jnp.dot(tok_rows, w_up, preferred_element_type=jnp.float32)
    sigmoid_gate = jax.nn.sigmoid(gate_pre)
    gate_act = gate_pre * sigmoid_gate
    hidden = (gate_act * up_pre).astype(jnp.bfloat16)
    d_hidden = jnp.dot(grad_rows, w_down, preferred_element_type=jnp.float32)
    d_gate = (d_hidden * up_pre * sigmoid_gate * (1.0 + gate_pre * (1.0 - sigmoid_gate))).astype(
        jnp.bfloat16
    )
    d_up = (d_hidden * gate_act).astype(jnp.bfloat16)
    grad_tok = (contract_cols(d_gate, w_gate) + contract_cols(d_up, w_up)).astype(jnp.bfloat16)
    summed = reduce_over_dp(
        tok_rows, grad_rows, jnp.concatenate([d_gate, d_up], axis=1), hidden
    )
    return (grad_tok, summed / lax.axis_size("dp"))


def reduce_over_dp(tok_rows, grad_rows, d_both, hidden):
    n = lax.axis_size("dp")
    nx = 2
    ny = n // nx
    index = lax.axis_index("dp")
    xh = index // ny
    y = index % ny
    rows, width = tok_rows.shape
    cols = hidden.shape[1]
    lane = 128
    blocks = width // lane // nx
    tok_view = tok_rows.reshape(rows, nx, blocks, lane)
    grad_view = grad_rows.reshape(rows, nx, blocks, lane)

    def chunk(c, h):
        b = c * 2 + h
        tok_part = lax.dynamic_index_in_dim(tok_view, b, axis=2, keepdims=False)
        grad_part = lax.dynamic_index_in_dim(grad_view, b, axis=2, keepdims=False)
        first = contract_rows(d_both, tok_part.reshape(rows, nx * lane))
        second = contract_rows(hidden, grad_part.reshape(rows, nx * lane))
        return jnp.concatenate([first, second], axis=0)

    fwd = [(a * ny + b, a * ny + (b + 1) % ny) for a in range(nx) for b in range(ny)]
    bwd = [(a * ny + b, a * ny + (b - 1) % ny) for a in range(nx) for b in range(ny)]
    acc_f = chunk((y + ny - 1) % ny, 0)
    acc_b = chunk((y + 1) % ny, 1)
    for s in range(ny - 1):
        recv_f = lax.ppermute(acc_f.astype(jnp.bfloat16), "dp", fwd)
        recv_b = lax.ppermute(acc_b.astype(jnp.bfloat16), "dp", bwd)
        acc_f = recv_f.astype(jnp.float32) + chunk((y + 2 * ny - 2 - s) % ny, 0)
        acc_b = recv_b.astype(jnp.float32) + chunk((y + 2 + s) % ny, 1)
    acc = jnp.stack([acc_f, acc_b], axis=1).reshape(-1, 2, nx, lane)
    mine = lax.dynamic_index_in_dim(acc, xh, axis=2, keepdims=False)
    other = lax.dynamic_index_in_dim(acc, 1 - xh, axis=2, keepdims=False)
    across = [(a * ny + b, (1 - a) * ny + b) for a in range(nx) for b in range(ny)]
    got = lax.ppermute(other.astype(jnp.bfloat16), "dp", across)
    total = (mine + got.astype(jnp.float32)).reshape(3, cols, 2 * lane)
    return jnp.transpose(total, (0, 2, 1))


def shards(tokens, cotangent, gate_weight, up_weight, down_weight, counts, seg_ids, pair_side):
    weights = token_weights(counts, seg_ids, pair_side)
    upstream = (cotangent.astype(jnp.float32) * weights[..., None]).astype(jnp.bfloat16)
    width = tokens.shape[-1]
    tok_rows = tokens.reshape(-1, width)
    grad_rows = upstream.reshape(-1, width)
    moved_rows, moved_grads = shifted((tok_rows, grad_rows), "blk", 1)
    grad_moved, panel_grads = backward_core(
        moved_rows, moved_grads, gate_weight, up_weight, down_weight
    )
    grad_tok = shifted(grad_moved, "blk", -1)
    return (grad_tok.reshape(tokens.shape), panel_grads)


def solution(mesh):
    placed = (
        P("dp", "blk", None, None),
        P("dp", "blk", None, None),
        P(None, "blk"),
        P(None, "blk"),
        P(None, "blk"),
        P("dp", "blk"),
        P("dp", "blk", None),
        P("dp", "blk", None),
    )
    return jax.shard_map(
        shards,
        mesh=mesh,
        in_specs=placed,
        out_specs=(P("dp", "blk", None, None), P(None, "dp", "blk")),
        check_vma=False,
    )
```

```python
import jax
import jax.numpy as jnp
from jax import lax
from jax.sharding import PartitionSpec as P

CAP = 128
SEQS = 4


def shifted(block, axis, distance):
    devices = range(lax.axis_size(axis))
    route = [((i - distance) % len(devices), i) for i in devices]
    return lax.ppermute(block, axis, route)


def token_weights(counts, seg_ids, pair_side):
    positions = jnp.arange(seg_ids.shape[-1], dtype=jnp.int32)
    valid_rows = positions[None, None, :] < counts[:, :, None]
    member = (seg_ids[..., None] == jnp.arange(SEQS, dtype=jnp.int32)) & valid_rows[..., None]
    member_f = member.astype(jnp.float32)
    length = jnp.sum(member_f, axis=2)
    half_span = jnp.float32(CAP) / jnp.float32(SEQS)
    seq_weight = (2.0 * pair_side.astype(jnp.float32) - 1.0) * half_span / (length + half_span)
    return jnp.sum(member_f * seq_weight[:, :, None, :], axis=3)


def contract_rows(left, right):
    return lax.dot_general(
        left, right, (((0,), (0,)), ((), ())), preferred_element_type=jnp.float32
    )


def contract_cols(left, right):
    return lax.dot_general(
        left, right, (((1,), (1,)), ((), ())), preferred_element_type=jnp.float32
    )


def backward_core(tok_rows, grad_rows, w_gate, w_up, w_down):
    n = lax.axis_size("dp")
    nx = 2
    ny = n // nx
    xh = lax.axis_index("dp") // ny
    across = [(a * ny + b, (1 - a) * ny + b) for a in range(nx) for b in range(ny)]
    rows, width = tok_rows.shape
    tok_halves = tok_rows.reshape(rows, nx, width // nx)
    grad_halves = grad_rows.reshape(rows, nx, width // nx)
    tok_mine = lax.dynamic_index_in_dim(tok_halves, xh, axis=1, keepdims=False)
    grad_mine = lax.dynamic_index_in_dim(grad_halves, xh, axis=1, keepdims=False)
    tok_other = lax.dynamic_index_in_dim(tok_halves, 1 - xh, axis=1, keepdims=False)
    grad_other = lax.dynamic_index_in_dim(grad_halves, 1 - xh, axis=1, keepdims=False)
    tok_peer, grad_peer = lax.ppermute((tok_other, grad_other), "dp", across)

    gate_pre = jnp.dot(tok_rows, w_gate, preferred_element_type=jnp.float32)
    up_pre = jnp.dot(tok_rows, w_up, preferred_element_type=jnp.float32)
    sigmoid_gate = jax.nn.sigmoid(gate_pre)
    gate_act = gate_pre * sigmoid_gate
    hidden = (gate_act * up_pre).astype(jnp.bfloat16)
    d_hidden = jnp.dot(grad_rows, w_down, preferred_element_type=jnp.float32)
    d_gate = (d_hidden * up_pre * sigmoid_gate * (1.0 + gate_pre * (1.0 - sigmoid_gate))).astype(
        jnp.bfloat16
    )
    d_up = (d_hidden * gate_act).astype(jnp.bfloat16)
    grad_tok = (contract_cols(d_gate, w_gate) + contract_cols(d_up, w_up)).astype(jnp.bfloat16)
    mixed = jnp.concatenate([d_gate, d_up, hidden], axis=1)
    mixed_peer = lax.ppermute(mixed, "dp", across)
    mixed_all = jnp.concatenate([mixed, mixed_peer], axis=0)
    tok_all = jnp.concatenate([tok_mine, tok_peer], axis=0)
    grad_all = jnp.concatenate([grad_mine, grad_peer], axis=0)
    summed = reduce_over_y(tok_all, grad_all, mixed_all, hidden.shape[1])
    return (grad_tok, summed / n)


def reduce_over_y(tok_all, grad_all, mixed_all, cols):
    n = lax.axis_size("dp")
    nx = 2
    ny = n // nx
    y = lax.axis_index("dp") % ny
    rows, width = tok_all.shape
    lane = width // ny // 2
    tok_view = tok_all.reshape(rows, ny * 2, lane)
    grad_view = grad_all.reshape(rows, ny * 2, lane)
    d_both = mixed_all[:, : 2 * cols]
    hidden = mixed_all[:, 2 * cols :]

    def chunk(c, h):
        b = c * 2 + h
        tok_part = lax.dynamic_index_in_dim(tok_view, b, axis=1, keepdims=False)
        grad_part = lax.dynamic_index_in_dim(grad_view, b, axis=1, keepdims=False)
        first = contract_rows(d_both, tok_part)
        second = contract_rows(hidden, grad_part)
        return jnp.concatenate([first, second], axis=0)

    fwd = [(a * ny + b, a * ny + (b + 1) % ny) for a in range(nx) for b in range(ny)]
    bwd = [(a * ny + b, a * ny + (b - 1) % ny) for a in range(nx) for b in range(ny)]
    acc_f = chunk((y + ny - 1) % ny, 0)
    acc_b = chunk((y + 1) % ny, 1)
    for s in range(ny - 1):
        recv_f = lax.ppermute(acc_f.astype(jnp.bfloat16), "dp", fwd)
        recv_b = lax.ppermute(acc_b.astype(jnp.bfloat16), "dp", bwd)
        acc_f = recv_f.astype(jnp.float32) + chunk((y + 2 * ny - 2 - s) % ny, 0)
        acc_b = recv_b.astype(jnp.float32) + chunk((y + 2 + s) % ny, 1)
    total = jnp.concatenate([acc_f, acc_b], axis=1).reshape(3, cols, 2 * lane)
    return jnp.transpose(total, (0, 2, 1))


def shards(tokens, cotangent, gate_weight, up_weight, down_weight, counts, seg_ids, pair_side):
    weights = token_weights(counts, seg_ids, pair_side)
    upstream = (cotangent.astype(jnp.float32) * weights[..., None]).astype(jnp.bfloat16)
    width = tokens.shape[-1]
    tok_rows = tokens.reshape(-1, width)
    grad_rows = upstream.reshape(-1, width)
    moved_rows, moved_grads = shifted((tok_rows, grad_rows), "blk", 1)
    grad_moved, panel_grads = backward_core(
        moved_rows, moved_grads, gate_weight, up_weight, down_weight
    )
    grad_tok = shifted(grad_moved, "blk", -1)
    return (grad_tok.reshape(tokens.shape), panel_grads)


def solution(mesh):
    placed = (
        P("dp", "blk", None, None),
        P("dp", "blk", None, None),
        P(None, "blk"),
        P(None, "blk"),
        P(None, "blk"),
        P("dp", "blk"),
        P("dp", "blk", None),
        P("dp", "blk", None),
    )
    return jax.shard_map(
        shards,
        mesh=mesh,
        in_specs=placed,
        out_specs=(P("dp", "blk", None, None), P(None, "dp", "blk")),
        check_vma=False,
    )
```

```python
import jax
import jax.numpy as jnp
from jax import lax
from jax.sharding import PartitionSpec as P

CAP = 128
SEQS = 4


def shifted(block, axis, distance):
    devices = range(lax.axis_size(axis))
    route = [((i - distance) % len(devices), i) for i in devices]
    return lax.ppermute(block, axis, route)


def token_weights(counts, seg_ids, pair_side):
    positions = jnp.arange(seg_ids.shape[-1], dtype=jnp.int32)
    valid_rows = positions[None, None, :] < counts[:, :, None]
    member = (seg_ids[..., None] == jnp.arange(SEQS, dtype=jnp.int32)) & valid_rows[..., None]
    member_f = member.astype(jnp.float32)
    length = jnp.sum(member_f, axis=2)
    half_span = jnp.float32(CAP) / jnp.float32(SEQS)
    seq_weight = (2.0 * pair_side.astype(jnp.float32) - 1.0) * half_span / (length + half_span)
    return jnp.sum(member_f * seq_weight[:, :, None, :], axis=3)


def contract_rows(left, right):
    return lax.dot_general(
        left, right, (((0,), (0,)), ((), ())), preferred_element_type=jnp.float32
    )


def contract_cols(left, right):
    return lax.dot_general(
        left, right, (((1,), (1,)), ((), ())), preferred_element_type=jnp.float32
    )


def backward_core(tok_rows, grad_rows, tok_peer, grad_peer, w_gate, w_up, w_down):
    n = lax.axis_size("dp")
    nx = 2
    ny = n // nx
    xh = lax.axis_index("dp") // ny
    across = [(a * ny + b, (1 - a) * ny + b) for a in range(nx) for b in range(ny)]
    rows, width = tok_rows.shape
    tok_halves = tok_rows.reshape(rows, nx, width // nx)
    grad_halves = grad_rows.reshape(rows, nx, width // nx)
    tok_mine = lax.dynamic_index_in_dim(tok_halves, xh, axis=1, keepdims=False)
    grad_mine = lax.dynamic_index_in_dim(grad_halves, xh, axis=1, keepdims=False)

    gate_pre = jnp.dot(tok_rows, w_gate, preferred_element_type=jnp.float32)
    up_pre = jnp.dot(tok_rows, w_up, preferred_element_type=jnp.float32)
    sigmoid_gate = jax.nn.sigmoid(gate_pre)
    gate_act = gate_pre * sigmoid_gate
    hidden = (gate_act * up_pre).astype(jnp.bfloat16)
    d_hidden = jnp.dot(grad_rows, w_down, preferred_element_type=jnp.float32)
    d_gate = (d_hidden * up_pre * sigmoid_gate * (1.0 + gate_pre * (1.0 - sigmoid_gate))).astype(
        jnp.bfloat16
    )
    d_up = (d_hidden * gate_act).astype(jnp.bfloat16)
    grad_tok = (contract_cols(d_gate, w_gate) + contract_cols(d_up, w_up)).astype(jnp.bfloat16)
    mixed = jnp.concatenate([d_gate, d_up, hidden], axis=1)
    mixed_peer = lax.ppermute(mixed, "dp", across)
    mixed_all = jnp.concatenate([mixed, mixed_peer], axis=0)
    tok_all = jnp.concatenate([tok_mine, tok_peer], axis=0)
    grad_all = jnp.concatenate([grad_mine, grad_peer], axis=0)
    summed = reduce_over_y(tok_all, grad_all, mixed_all, hidden.shape[1])
    return (grad_tok, summed / n)


def reduce_over_y(tok_all, grad_all, mixed_all, cols):
    n = lax.axis_size("dp")
    nx = 2
    ny = n // nx
    y = lax.axis_index("dp") % ny
    rows, width = tok_all.shape
    lane = width // ny // 2
    tok_view = tok_all.reshape(rows, ny * 2, lane)
    grad_view = grad_all.reshape(rows, ny * 2, lane)
    d_both = mixed_all[:, : 2 * cols]
    hidden = mixed_all[:, 2 * cols :]

    def chunk(c, h):
        b = c * 2 + h
        tok_part = lax.dynamic_index_in_dim(tok_view, b, axis=1, keepdims=False)
        grad_part = lax.dynamic_index_in_dim(grad_view, b, axis=1, keepdims=False)
        first = contract_rows(d_both, tok_part)
        second = contract_rows(hidden, grad_part)
        return jnp.concatenate([first, second], axis=0)

    fwd = [(a * ny + b, a * ny + (b + 1) % ny) for a in range(nx) for b in range(ny)]
    bwd = [(a * ny + b, a * ny + (b - 1) % ny) for a in range(nx) for b in range(ny)]
    acc_f = chunk((y + ny - 1) % ny, 0)
    acc_b = chunk((y + 1) % ny, 1)
    for s in range(ny - 1):
        recv_f = lax.ppermute(acc_f.astype(jnp.bfloat16), "dp", fwd)
        recv_b = lax.ppermute(acc_b.astype(jnp.bfloat16), "dp", bwd)
        acc_f = recv_f.astype(jnp.float32) + chunk((y + 2 * ny - 2 - s) % ny, 0)
        acc_b = recv_b.astype(jnp.float32) + chunk((y + 2 + s) % ny, 1)
    total = jnp.concatenate([acc_f, acc_b], axis=1).reshape(3, cols, 2 * lane)
    return jnp.transpose(total, (0, 2, 1))


def shards(tokens, cotangent, gate_weight, up_weight, down_weight, counts, seg_ids, pair_side):
    weights = token_weights(counts, seg_ids, pair_side)
    upstream = (cotangent.astype(jnp.float32) * weights[..., None]).astype(jnp.bfloat16)
    width = tokens.shape[-1]
    tok_rows = tokens.reshape(-1, width)
    grad_rows = upstream.reshape(-1, width)
    moved_rows, moved_grads = shifted((tok_rows, grad_rows), "blk", 1)
    n = lax.axis_size("dp")
    nb = lax.axis_size("blk")
    ny = n // 2
    xh = lax.axis_index("dp") // ny
    halves = (tok_rows.reshape(tok_rows.shape[0], 2, -1), grad_rows.reshape(grad_rows.shape[0], 2, -1))
    other = tuple(lax.dynamic_index_in_dim(h, 1 - xh, axis=1, keepdims=False) for h in halves)
    diagonal = [
        (d * nb + j, ((d + ny) % n) * nb + (j + 1) % nb) for d in range(n) for j in range(nb)
    ]
    tok_peer, grad_peer = lax.ppermute(other, ("dp", "blk"), diagonal)
    grad_moved, panel_grads = backward_core(
        moved_rows, moved_grads, tok_peer, grad_peer, gate_weight, up_weight, down_weight
    )
    grad_tok = shifted(grad_moved, "blk", -1)
    return (grad_tok.reshape(tokens.shape), panel_grads)


def solution(mesh):
    placed = (
        P("dp", "blk", None, None),
        P("dp", "blk", None, None),
        P(None, "blk"),
        P(None, "blk"),
        P(None, "blk"),
        P("dp", "blk"),
        P("dp", "blk", None),
        P("dp", "blk", None),
    )
    return jax.shard_map(
        shards,
        mesh=mesh,
        in_specs=placed,
        out_specs=(P("dp", "blk", None, None), P(None, "dp", "blk")),
        check_vma=False,
    )
```

```python
import jax
import jax.numpy as jnp
from jax import lax
from jax.sharding import PartitionSpec as P

CAP = 128
SEQS = 4


def shifted(block, axis, distance):
    devices = range(lax.axis_size(axis))
    route = [((i - distance) % len(devices), i) for i in devices]
    return lax.ppermute(block, axis, route)


def token_weights(counts, seg_ids, pair_side):
    positions = jnp.arange(seg_ids.shape[-1], dtype=jnp.int32)
    valid_rows = positions[None, None, :] < counts[:, :, None]
    member = (seg_ids[..., None] == jnp.arange(SEQS, dtype=jnp.int32)) & valid_rows[..., None]
    member_f = member.astype(jnp.float32)
    length = jnp.sum(member_f, axis=2)
    half_span = jnp.float32(CAP) / jnp.float32(SEQS)
    seq_weight = (2.0 * pair_side.astype(jnp.float32) - 1.0) * half_span / (length + half_span)
    return jnp.sum(member_f * seq_weight[:, :, None, :], axis=3)


def contract_rows(left, right):
    return lax.dot_general(
        left, right, (((0,), (0,)), ((), ())), preferred_element_type=jnp.float32
    )


def contract_cols(left, right):
    return lax.dot_general(
        left, right, (((1,), (1,)), ((), ())), preferred_element_type=jnp.float32
    )


def backward_core(tok_rows, grad_rows, tok_peer, grad_peer, w_gate, w_up, w_down):
    n = lax.axis_size("dp")
    nx = 2
    ny = n // nx
    xh = lax.axis_index("dp") // ny
    across = [(a * ny + b, (1 - a) * ny + b) for a in range(nx) for b in range(ny)]
    rows, width = tok_rows.shape
    tok_halves = tok_rows.reshape(rows, nx, width // nx)
    grad_halves = grad_rows.reshape(rows, nx, width // nx)
    tok_mine = lax.dynamic_index_in_dim(tok_halves, xh, axis=1, keepdims=False)
    grad_mine = lax.dynamic_index_in_dim(grad_halves, xh, axis=1, keepdims=False)

    gate_pre = jnp.dot(tok_rows, w_gate, preferred_element_type=jnp.float32)
    up_pre = jnp.dot(tok_rows, w_up, preferred_element_type=jnp.float32)
    sigmoid_gate = jax.nn.sigmoid(gate_pre)
    gate_act = gate_pre * sigmoid_gate
    hidden = (gate_act * up_pre).astype(jnp.bfloat16)
    d_hidden = jnp.dot(grad_rows, w_down, preferred_element_type=jnp.float32)
    d_gate = (d_hidden * up_pre * sigmoid_gate * (1.0 + gate_pre * (1.0 - sigmoid_gate))).astype(
        jnp.bfloat16
    )
    d_up = (d_hidden * gate_act).astype(jnp.bfloat16)
    mixed = jnp.concatenate([d_gate, d_up, hidden], axis=1)
    mixed_peer = lax.ppermute(mixed, "dp", across)
    mixed_all = jnp.concatenate([mixed, mixed_peer], axis=0)
    tok_all = jnp.concatenate([tok_mine, tok_peer], axis=0)
    grad_all = jnp.concatenate([grad_mine, grad_peer], axis=0)
    def late(d_gate, d_up):
        return (contract_cols(d_gate, w_gate) + contract_cols(d_up, w_up)).astype(jnp.bfloat16)

    summed, grad_tok = reduce_over_y(
        tok_all, grad_all, mixed_all, hidden.shape[1], late, (d_gate, d_up)
    )
    return (grad_tok, summed / n)


def reduce_over_y(tok_all, grad_all, mixed_all, cols, late, late_args):
    n = lax.axis_size("dp")
    nx = 2
    ny = n // nx
    y = lax.axis_index("dp") % ny
    rows, width = tok_all.shape
    lane = width // ny // 2
    tok_view = tok_all.reshape(rows, ny * 2, lane)
    grad_view = grad_all.reshape(rows, ny * 2, lane)
    d_both = mixed_all[:, : 2 * cols]
    hidden = mixed_all[:, 2 * cols :]

    def chunk(c, h):
        b = c * 2 + h
        tok_part = lax.dynamic_index_in_dim(tok_view, b, axis=1, keepdims=False)
        grad_part = lax.dynamic_index_in_dim(grad_view, b, axis=1, keepdims=False)
        first = contract_rows(d_both, tok_part)
        second = contract_rows(hidden, grad_part)
        return jnp.concatenate([first, second], axis=0)

    fwd = [(a * ny + b, a * ny + (b + 1) % ny) for a in range(nx) for b in range(ny)]
    bwd = [(a * ny + b, a * ny + (b - 1) % ny) for a in range(nx) for b in range(ny)]
    acc_f = chunk((y + ny - 1) % ny, 0)
    acc_b = chunk((y + 1) % ny, 1)
    for s in range(ny - 1):
        recv_f = lax.ppermute(acc_f.astype(jnp.bfloat16), "dp", fwd)
        recv_b = lax.ppermute(acc_b.astype(jnp.bfloat16), "dp", bwd)
        if s == 0:
            recv_f, recv_b, late_args = lax.optimization_barrier((recv_f, recv_b, late_args))
            late_out = late(*late_args)
        acc_f = recv_f.astype(jnp.float32) + chunk((y + 2 * ny - 2 - s) % ny, 0)
        acc_b = recv_b.astype(jnp.float32) + chunk((y + 2 + s) % ny, 1)
    total = jnp.concatenate([acc_f, acc_b], axis=1).reshape(3, cols, 2 * lane)
    return jnp.transpose(total, (0, 2, 1)), late_out


def shards(tokens, cotangent, gate_weight, up_weight, down_weight, counts, seg_ids, pair_side):
    weights = token_weights(counts, seg_ids, pair_side)
    upstream = (cotangent.astype(jnp.float32) * weights[..., None]).astype(jnp.bfloat16)
    width = tokens.shape[-1]
    tok_rows = tokens.reshape(-1, width)
    grad_rows = upstream.reshape(-1, width)
    moved_rows, moved_grads = shifted((tok_rows, grad_rows), "blk", 1)
    n = lax.axis_size("dp")
    nb = lax.axis_size("blk")
    ny = n // 2
    xh = lax.axis_index("dp") // ny
    halves = (tok_rows.reshape(tok_rows.shape[0], 2, -1), grad_rows.reshape(grad_rows.shape[0], 2, -1))
    other = tuple(lax.dynamic_index_in_dim(h, 1 - xh, axis=1, keepdims=False) for h in halves)
    diagonal = [
        (d * nb + j, ((d + ny) % n) * nb + (j + 1) % nb) for d in range(n) for j in range(nb)
    ]
    tok_peer, grad_peer = lax.ppermute(other, ("dp", "blk"), diagonal)
    grad_moved, panel_grads = backward_core(
        moved_rows, moved_grads, tok_peer, grad_peer, gate_weight, up_weight, down_weight
    )
    grad_tok = shifted(grad_moved, "blk", -1)
    return (grad_tok.reshape(tokens.shape), panel_grads)


def solution(mesh):
    placed = (
        P("dp", "blk", None, None),
        P("dp", "blk", None, None),
        P(None, "blk"),
        P(None, "blk"),
        P(None, "blk"),
        P("dp", "blk"),
        P("dp", "blk", None),
        P("dp", "blk", None),
    )
    return jax.shard_map(
        shards,
        mesh=mesh,
        in_specs=placed,
        out_specs=(P("dp", "blk", None, None), P(None, "dp", "blk")),
        check_vma=False,
    )
```

```python
import jax
import jax.numpy as jnp
from jax import lax
from jax.sharding import PartitionSpec as P

CAP = 128
SEQS = 4


def shifted(block, axis, distance):
    devices = range(lax.axis_size(axis))
    route = [((i - distance) % len(devices), i) for i in devices]
    return lax.ppermute(block, axis, route)


def token_weights(counts, seg_ids, pair_side):
    positions = jnp.arange(seg_ids.shape[-1], dtype=jnp.int32)
    valid_rows = positions[None, None, :] < counts[:, :, None]
    member = (seg_ids[..., None] == jnp.arange(SEQS, dtype=jnp.int32)) & valid_rows[..., None]
    member_f = member.astype(jnp.float32)
    length = jnp.sum(member_f, axis=2)
    half_span = jnp.float32(CAP) / jnp.float32(SEQS)
    seq_weight = (2.0 * pair_side.astype(jnp.float32) - 1.0) * half_span / (length + half_span)
    return jnp.sum(member_f * seq_weight[:, :, None, :], axis=3)


def contract_rows(left, right):
    return lax.dot_general(
        left, right, (((0,), (0,)), ((), ())), preferred_element_type=jnp.float32
    )


def contract_cols(left, right):
    return lax.dot_general(
        left, right, (((1,), (1,)), ((), ())), preferred_element_type=jnp.float32
    )


def backward_core(tok_rows, grad_rows, tok_peer, grad_peer, w_gate, w_up, w_down):
    n = lax.axis_size("dp")
    nx = 2
    ny = n // nx
    xh = lax.axis_index("dp") // ny
    across = [(a * ny + b, (1 - a) * ny + b) for a in range(nx) for b in range(ny)]
    rows, width = tok_rows.shape
    tok_halves = tok_rows.reshape(rows, nx, width // nx)
    grad_halves = grad_rows.reshape(rows, nx, width // nx)
    tok_mine = lax.dynamic_index_in_dim(tok_halves, xh, axis=1, keepdims=False)
    grad_mine = lax.dynamic_index_in_dim(grad_halves, xh, axis=1, keepdims=False)

    gate_pre = jnp.dot(tok_rows, w_gate, preferred_element_type=jnp.float32)
    up_pre = jnp.dot(tok_rows, w_up, preferred_element_type=jnp.float32)
    sigmoid_gate = jax.nn.sigmoid(gate_pre)
    gate_act = gate_pre * sigmoid_gate
    hidden = (gate_act * up_pre).astype(jnp.bfloat16)
    d_hidden = jnp.dot(grad_rows, w_down, preferred_element_type=jnp.float32)
    d_gate = (d_hidden * up_pre * sigmoid_gate * (1.0 + gate_pre * (1.0 - sigmoid_gate))).astype(
        jnp.bfloat16
    )
    d_up = (d_hidden * gate_act).astype(jnp.bfloat16)
    mixed = jnp.concatenate([d_gate, d_up, hidden], axis=1)
    mixed_peer = lax.ppermute(mixed, "dp", across)
    mixed_all = jnp.concatenate([mixed, mixed_peer], axis=0)
    tok_all = jnp.concatenate([tok_mine, tok_peer], axis=0)
    grad_all = jnp.concatenate([grad_mine, grad_peer], axis=0)

    def late(d_gate, d_up):
        return (contract_cols(d_gate, w_gate) + contract_cols(d_up, w_up)).astype(jnp.bfloat16)

    summed, grad_tok = reduce_over_y(
        tok_all, grad_all, mixed_all, hidden.shape[1], late, (d_gate, d_up)
    )
    return (grad_tok, summed / n)


def reduce_over_y(tok_all, grad_all, mixed_all, cols, late, late_args):
    n = lax.axis_size("dp")
    nx = 2
    ny = n // nx
    y = lax.axis_index("dp") % ny
    rows, width = tok_all.shape
    lane = width // ny // 2
    tok_view = tok_all.reshape(rows, ny * 2, lane)
    grad_view = grad_all.reshape(rows, ny * 2, lane)
    d_both = mixed_all[:, : 2 * cols]
    hidden = mixed_all[:, 2 * cols :]

    def chunk(c, h):
        b = c * 2 + h
        tok_part = lax.dynamic_index_in_dim(tok_view, b, axis=1, keepdims=False)
        grad_part = lax.dynamic_index_in_dim(grad_view, b, axis=1, keepdims=False)
        first = contract_rows(d_both, tok_part)
        second = contract_rows(hidden, grad_part)
        return jnp.concatenate([first, second], axis=0)

    fwd = [(a * ny + b, a * ny + (b + 1) % ny) for a in range(nx) for b in range(ny)]
    bwd = [(a * ny + b, a * ny + (b - 1) % ny) for a in range(nx) for b in range(ny)]
    acc_f = chunk((y + ny - 1) % ny, 0)
    acc_b = chunk((y + 1) % ny, 1)
    for s in range(ny - 1):
        recv_f = lax.ppermute(acc_f.astype(jnp.bfloat16), "dp", fwd)
        recv_b = lax.ppermute(acc_b.astype(jnp.bfloat16), "dp", bwd)
        if s == 0:
            recv_f, recv_b, late_args = lax.optimization_barrier((recv_f, recv_b, late_args))
            late_out = late(*late_args)
        acc_f = recv_f.astype(jnp.float32) + chunk((y + 2 * ny - 2 - s) % ny, 0)
        acc_b = recv_b.astype(jnp.float32) + chunk((y + 2 + s) % ny, 1)
    total = jnp.concatenate([acc_f, acc_b], axis=1).reshape(3, cols, 2 * lane)
    return jnp.transpose(total, (0, 2, 1)), late_out


def shards_body(tokens, cotangent, gate_weight, up_weight, down_weight, counts, seg_ids, pair_side):
    weights = token_weights(counts, seg_ids, pair_side)
    upstream = (cotangent.astype(jnp.float32) * weights[..., None]).astype(jnp.bfloat16)
    width = tokens.shape[-1]
    tok_rows = tokens.reshape(-1, width)
    grad_rows = upstream.reshape(-1, width)
    moved_rows, moved_grads = shifted((tok_rows, grad_rows), "blk", 1)
    n = lax.axis_size("dp")
    nb = lax.axis_size("blk")
    ny = n // 2
    xh = lax.axis_index("dp") // ny
    halves = (tok_rows.reshape(tok_rows.shape[0], 2, -1), grad_rows.reshape(grad_rows.shape[0], 2, -1))
    other = tuple(lax.dynamic_index_in_dim(h, 1 - xh, axis=1, keepdims=False) for h in halves)
    diagonal = [
        (d * nb + j, ((d + ny) % n) * nb + (j + 1) % nb) for d in range(n) for j in range(nb)
    ]
    other, moved_rows, moved_grads = lax.optimization_barrier((other, moved_rows, moved_grads))
    tok_peer, grad_peer = lax.ppermute(other, ("dp", "blk"), diagonal)
    grad_moved, panel_grads = backward_core(
        moved_rows, moved_grads, tok_peer, grad_peer, gate_weight, up_weight, down_weight
    )
    grad_tok = shifted(grad_moved, "blk", -1)
    return (grad_tok.reshape(tokens.shape), panel_grads)


def solution(mesh):
    placed = (
        P("dp", "blk", None, None),
        P("dp", "blk", None, None),
        P(None, "blk"),
        P(None, "blk"),
        P(None, "blk"),
        P("dp", "blk"),
        P("dp", "blk", None),
        P("dp", "blk", None),
    )
    return jax.shard_map(
        shards_body,
        mesh=mesh,
        in_specs=placed,
        out_specs=(P("dp", "blk", None, None), P(None, "dp", "blk")),
        check_vma=False,
    )
```

```python
import jax
import jax.numpy as jnp
from jax import lax
from jax.sharding import PartitionSpec as P

CAP = 128
SEQS = 4


def shifted(block, axis, distance):
    devices = range(lax.axis_size(axis))
    route = [((i - distance) % len(devices), i) for i in devices]
    return lax.ppermute(block, axis, route)


def token_weights(counts, seg_ids, pair_side):
    positions = jnp.arange(seg_ids.shape[-1], dtype=jnp.int32)
    valid_rows = positions[None, None, :] < counts[:, :, None]
    member = (seg_ids[..., None] == jnp.arange(SEQS, dtype=jnp.int32)) & valid_rows[..., None]
    member_f = member.astype(jnp.float32)
    length = jnp.sum(member_f, axis=2)
    half_span = jnp.float32(CAP) / jnp.float32(SEQS)
    seq_weight = (2.0 * pair_side.astype(jnp.float32) - 1.0) * half_span / (length + half_span)
    return jnp.sum(member_f * seq_weight[:, :, None, :], axis=3)


def contract_rows(left, right):
    return lax.dot_general(
        left, right, (((0,), (0,)), ((), ())), preferred_element_type=jnp.float32
    )


def contract_cols(left, right):
    return lax.dot_general(
        left, right, (((1,), (1,)), ((), ())), preferred_element_type=jnp.float32
    )


def backward_core(tok_rows, grad_rows, tok_peer, grad_peer, w_gate, w_up, w_down):
    n = lax.axis_size("dp")
    nx = 2
    ny = n // nx
    xh = lax.axis_index("dp") // ny
    across = [(a * ny + b, (1 - a) * ny + b) for a in range(nx) for b in range(ny)]
    rows, width = tok_rows.shape
    tok_halves = tok_rows.reshape(rows, nx, width // nx)
    grad_halves = grad_rows.reshape(rows, nx, width // nx)
    tok_mine = lax.dynamic_index_in_dim(tok_halves, xh, axis=1, keepdims=False)
    grad_mine = lax.dynamic_index_in_dim(grad_halves, xh, axis=1, keepdims=False)

    gate_pre = jnp.dot(tok_rows, w_gate, preferred_element_type=jnp.float32)
    up_pre = jnp.dot(tok_rows, w_up, preferred_element_type=jnp.float32)
    sigmoid_gate = jax.nn.sigmoid(gate_pre)
    gate_act = gate_pre * sigmoid_gate
    hidden = (gate_act * up_pre).astype(jnp.bfloat16)
    d_hidden = jnp.dot(grad_rows, w_down, preferred_element_type=jnp.float32)
    d_gate = (d_hidden * up_pre * sigmoid_gate * (1.0 + gate_pre * (1.0 - sigmoid_gate))).astype(
        jnp.bfloat16
    )
    d_up = (d_hidden * gate_act).astype(jnp.bfloat16)
    mixed = jnp.concatenate([d_gate, d_up, hidden], axis=1)
    mixed_peer = lax.ppermute(mixed, "dp", across)
    mixed_all = jnp.concatenate([mixed, mixed_peer], axis=0)
    tok_all = jnp.concatenate([tok_mine, tok_peer], axis=0)
    grad_all = jnp.concatenate([grad_mine, grad_peer], axis=0)
    def late(d_gate, d_up):
        return (contract_cols(d_gate, w_gate) + contract_cols(d_up, w_up)).astype(jnp.bfloat16)

    summed, grad_tok = reduce_over_y(
        tok_all, grad_all, mixed_all, hidden.shape[1], late, (d_gate, d_up)
    )
    return (grad_tok, summed / n)


def reduce_over_y(tok_all, grad_all, mixed_all, cols, late, late_args):
    n = lax.axis_size("dp")
    nx = 2
    ny = n // nx
    y = lax.axis_index("dp") % ny
    rows, width = tok_all.shape
    lane = width // ny // 2
    tok_view = tok_all.reshape(rows, ny * 2, lane)
    grad_view = grad_all.reshape(rows, ny * 2, lane)
    d_both = mixed_all[:, : 2 * cols]
    hidden = mixed_all[:, 2 * cols :]

    def chunk(c, h):
        b = c * 2 + h
        tok_part = lax.dynamic_index_in_dim(tok_view, b, axis=1, keepdims=False)
        grad_part = lax.dynamic_index_in_dim(grad_view, b, axis=1, keepdims=False)
        first = contract_rows(d_both, tok_part)
        second = contract_rows(hidden, grad_part)
        return jnp.concatenate([first, second], axis=0)

    fwd = [(a * ny + b, a * ny + (b + 1) % ny) for a in range(nx) for b in range(ny)]
    bwd = [(a * ny + b, a * ny + (b - 1) % ny) for a in range(nx) for b in range(ny)]
    acc_f = chunk((y + ny - 1) % ny, 0)
    acc_b = chunk((y + 1) % ny, 1)
    for s in range(ny - 1):
        recv_f = lax.ppermute(acc_f.astype(jnp.bfloat16), "dp", fwd)
        recv_b = lax.ppermute(acc_b.astype(jnp.bfloat16), "dp", bwd)
        if s == 0:
            recv_f, recv_b, late_args = lax.optimization_barrier((recv_f, recv_b, late_args))
            late_out = late(*late_args)
        acc_f = recv_f.astype(jnp.float32) + chunk((y + 2 * ny - 2 - s) % ny, 0)
        acc_b = recv_b.astype(jnp.float32) + chunk((y + 2 + s) % ny, 1)
    total = jnp.concatenate([acc_f, acc_b], axis=1).reshape(3, cols, 2 * lane)
    return jnp.transpose(total, (0, 2, 1)), late_out


def shards(tokens, cotangent, gate_weight, up_weight, down_weight, counts, seg_ids, pair_side):
    weights = token_weights(counts, seg_ids, pair_side)
    upstream = (cotangent.astype(jnp.float32) * weights[..., None]).astype(jnp.bfloat16)
    width = tokens.shape[-1]
    tok_rows = tokens.reshape(-1, width)
    grad_rows = upstream.reshape(-1, width)
    moved_rows, moved_grads = shifted(jnp.stack([tok_rows, grad_rows]), "blk", 1)
    n = lax.axis_size("dp")
    nb = lax.axis_size("blk")
    ny = n // 2
    xh = lax.axis_index("dp") // ny
    halves = (tok_rows.reshape(tok_rows.shape[0], 2, -1), grad_rows.reshape(grad_rows.shape[0], 2, -1))
    other = tuple(lax.dynamic_index_in_dim(h, 1 - xh, axis=1, keepdims=False) for h in halves)
    diagonal = [
        (d * nb + j, ((d + ny) % n) * nb + (j + 1) % nb) for d in range(n) for j in range(nb)
    ]
    tok_peer, grad_peer = lax.ppermute(jnp.stack(other), ("dp", "blk"), diagonal)
    grad_moved, panel_grads = backward_core(
        moved_rows, moved_grads, tok_peer, grad_peer, gate_weight, up_weight, down_weight
    )
    grad_tok = shifted(grad_moved, "blk", -1)
    return (grad_tok.reshape(tokens.shape), panel_grads)


def solution(mesh):
    placed = (
        P("dp", "blk", None, None),
        P("dp", "blk", None, None),
        P(None, "blk"),
        P(None, "blk"),
        P(None, "blk"),
        P("dp", "blk"),
        P("dp", "blk", None),
        P("dp", "blk", None),
    )
    return jax.shard_map(
        shards,
        mesh=mesh,
        in_specs=placed,
        out_specs=(P("dp", "blk", None, None), P(None, "dp", "blk")),
        check_vma=False,
    )
```

```python
import jax
import jax.numpy as jnp
from jax import lax
from jax.sharding import PartitionSpec as P

CAP = 128
SEQS = 4


def shifted(block, axis, distance):
    devices = range(lax.axis_size(axis))
    route = [((i - distance) % len(devices), i) for i in devices]
    return lax.ppermute(block, axis, route)


def token_weights(counts, seg_ids, pair_side):
    positions = jnp.arange(seg_ids.shape[-1], dtype=jnp.int32)
    valid_rows = positions[None, None, :] < counts[:, :, None]
    member = (seg_ids[..., None] == jnp.arange(SEQS, dtype=jnp.int32)) & valid_rows[..., None]
    member_f = member.astype(jnp.float32)
    length = jnp.sum(member_f, axis=2)
    half_span = jnp.float32(CAP) / jnp.float32(SEQS)
    seq_weight = (2.0 * pair_side.astype(jnp.float32) - 1.0) * half_span / (length + half_span)
    return jnp.sum(member_f * seq_weight[:, :, None, :], axis=3)


def contract_rows(left, right):
    return lax.dot_general(
        left, right, (((0,), (0,)), ((), ())), preferred_element_type=jnp.float32
    )


def contract_cols(left, right):
    return lax.dot_general(
        left, right, (((1,), (1,)), ((), ())), preferred_element_type=jnp.float32
    )


def backward_core(tok_rows, grad_rows, tok_peer, grad_peer, w_gate, w_up, w_down):
    n = lax.axis_size("dp")
    nx = 2
    ny = n // nx
    xh = lax.axis_index("dp") // ny
    across = [(a * ny + b, (1 - a) * ny + b) for a in range(nx) for b in range(ny)]
    rows, width = tok_rows.shape
    tok_halves = tok_rows.reshape(rows, nx, width // nx)
    grad_halves = grad_rows.reshape(rows, nx, width // nx)
    tok_mine = lax.dynamic_index_in_dim(tok_halves, xh, axis=1, keepdims=False)
    grad_mine = lax.dynamic_index_in_dim(grad_halves, xh, axis=1, keepdims=False)

    gate_pre = jnp.dot(tok_rows, w_gate, preferred_element_type=jnp.float32)
    up_pre = jnp.dot(tok_rows, w_up, preferred_element_type=jnp.float32)
    sigmoid_gate = jax.nn.sigmoid(gate_pre)
    gate_act = gate_pre * sigmoid_gate
    hidden = (gate_act * up_pre).astype(jnp.bfloat16)
    d_hidden = jnp.dot(grad_rows, w_down, preferred_element_type=jnp.float32)
    d_gate = (d_hidden * up_pre * sigmoid_gate * (1.0 + gate_pre * (1.0 - sigmoid_gate))).astype(
        jnp.bfloat16
    )
    d_up = (d_hidden * gate_act).astype(jnp.bfloat16)
    mixed = jnp.concatenate([d_gate, d_up, hidden], axis=1)
    mixed_peer = lax.ppermute(mixed, "dp", across)
    mixed_all = jnp.concatenate([mixed, mixed_peer], axis=0)
    tok_all = jnp.concatenate([tok_mine, tok_peer], axis=0)
    grad_all = jnp.concatenate([grad_mine, grad_peer], axis=0)
    def late(d_gate, d_up):
        return (contract_cols(d_gate, w_gate) + contract_cols(d_up, w_up)).astype(jnp.bfloat16)

    summed, grad_tok = reduce_over_y(
        tok_all, grad_all, mixed_all, hidden.shape[1], late, (d_gate, d_up)
    )
    return (grad_tok, summed)


def reduce_over_y(tok_all, grad_all, mixed_all, cols, late, late_args):
    n = lax.axis_size("dp")
    nx = 2
    ny = n // nx
    y = lax.axis_index("dp") % ny
    rows, width = tok_all.shape
    lane = width // ny // 2
    tok_view = tok_all.reshape(rows, ny * 2, lane)
    grad_view = grad_all.reshape(rows, ny * 2, lane)
    d_both = mixed_all[:, : 2 * cols]
    hidden = mixed_all[:, 2 * cols :]

    def chunk(c, h):
        b = c * 2 + h
        tok_part = lax.dynamic_index_in_dim(tok_view, b, axis=1, keepdims=False)
        grad_part = lax.dynamic_index_in_dim(grad_view, b, axis=1, keepdims=False)
        first = contract_rows(d_both, tok_part)
        second = contract_rows(hidden, grad_part)
        return jnp.concatenate([first, second], axis=0)

    fwd = [(a * ny + b, a * ny + (b + 1) % ny) for a in range(nx) for b in range(ny)]
    bwd = [(a * ny + b, a * ny + (b - 1) % ny) for a in range(nx) for b in range(ny)]
    acc_f = chunk((y + ny - 1) % ny, 0)
    acc_b = chunk((y + 1) % ny, 1)
    for s in range(ny - 1):
        recv_f = lax.ppermute(acc_f.astype(jnp.bfloat16), "dp", fwd)
        recv_b = lax.ppermute(acc_b.astype(jnp.bfloat16), "dp", bwd)
        if s == 0:
            recv_f, recv_b, late_args = lax.optimization_barrier((recv_f, recv_b, late_args))
            late_out = late(*late_args)
        scale = 1.0 / n if s == ny - 2 else 1.0
        acc_f = (recv_f.astype(jnp.float32) + chunk((y + 2 * ny - 2 - s) % ny, 0)) * scale
        acc_b = (recv_b.astype(jnp.float32) + chunk((y + 2 + s) % ny, 1)) * scale
    total = jnp.concatenate([acc_f, acc_b], axis=1).reshape(3, cols, 2 * lane)
    return jnp.transpose(total, (0, 2, 1)), late_out


def shards(tokens, cotangent, gate_weight, up_weight, down_weight, counts, seg_ids, pair_side):
    weights = token_weights(counts, seg_ids, pair_side)
    upstream = (cotangent.astype(jnp.float32) * weights[..., None]).astype(jnp.bfloat16)
    width = tokens.shape[-1]
    tok_rows = tokens.reshape(-1, width)
    grad_rows = upstream.reshape(-1, width)
    moved_rows, moved_grads = shifted((tok_rows, grad_rows), "blk", 1)
    n = lax.axis_size("dp")
    nb = lax.axis_size("blk")
    ny = n // 2
    xh = lax.axis_index("dp") // ny
    halves = (tok_rows.reshape(tok_rows.shape[0], 2, -1), grad_rows.reshape(grad_rows.shape[0], 2, -1))
    other = tuple(lax.dynamic_index_in_dim(h, 1 - xh, axis=1, keepdims=False) for h in halves)
    diagonal = [
        (d * nb + j, ((d + ny) % n) * nb + (j + 1) % nb) for d in range(n) for j in range(nb)
    ]
    tok_peer, grad_peer = lax.ppermute(other, ("dp", "blk"), diagonal)
    grad_moved, panel_grads = backward_core(
        moved_rows, moved_grads, tok_peer, grad_peer, gate_weight, up_weight, down_weight
    )
    grad_tok = shifted(grad_moved, "blk", -1)
    return (grad_tok.reshape(tokens.shape), panel_grads)


def solution(mesh):
    placed = (
        P("dp", "blk", None, None),
        P("dp", "blk", None, None),
        P(None, "blk"),
        P(None, "blk"),
        P(None, "blk"),
        P("dp", "blk"),
        P("dp", "blk", None),
        P("dp", "blk", None),
    )
    return jax.shard_map(
        shards,
        mesh=mesh,
        in_specs=placed,
        out_specs=(P("dp", "blk", None, None), P(None, "dp", "blk")),
        check_vma=False,
    )
```

```python
import jax
import jax.numpy as jnp
from jax import lax
from jax.sharding import PartitionSpec as P

CAP = 128
SEQS = 4


def shifted(block, axis, distance):
    devices = range(lax.axis_size(axis))
    route = [((i - distance) % len(devices), i) for i in devices]
    return lax.ppermute(block, axis, route)


def token_weights(counts, seg_ids, pair_side):
    positions = jnp.arange(seg_ids.shape[-1], dtype=jnp.int32)
    valid_rows = positions[None, None, :] < counts[:, :, None]
    member = (seg_ids[..., None] == jnp.arange(SEQS, dtype=jnp.int32)) & valid_rows[..., None]
    member_f = member.astype(jnp.float32)
    length = jnp.sum(member_f, axis=2)
    half_span = jnp.float32(CAP) / jnp.float32(SEQS)
    seq_weight = (2.0 * pair_side.astype(jnp.float32) - 1.0) * half_span / (length + half_span)
    return jnp.sum(member_f * seq_weight[:, :, None, :], axis=3)


def contract_rows(left, right):
    return lax.dot_general(
        left, right, (((0,), (0,)), ((), ())), preferred_element_type=jnp.float32
    )


def contract_cols(left, right):
    return lax.dot_general(
        left, right, (((1,), (1,)), ((), ())), preferred_element_type=jnp.float32
    )


def backward_core(tok_rows, grad_rows, tok_peer, grad_peer, w_gate, w_up, w_down):
    n = lax.axis_size("dp")
    nx = 2
    ny = n // nx
    xh = lax.axis_index("dp") // ny
    across = [(a * ny + b, (1 - a) * ny + b) for a in range(nx) for b in range(ny)]
    rows, width = tok_rows.shape
    tok_halves = tok_rows.reshape(rows, nx, width // nx)
    grad_halves = grad_rows.reshape(rows, nx, width // nx)
    tok_mine = lax.dynamic_index_in_dim(tok_halves, xh, axis=1, keepdims=False)
    grad_mine = lax.dynamic_index_in_dim(grad_halves, xh, axis=1, keepdims=False)

    gate_pre = jnp.dot(tok_rows, w_gate, preferred_element_type=jnp.float32)
    up_pre = jnp.dot(tok_rows, w_up, preferred_element_type=jnp.float32)
    sigmoid_gate = jax.nn.sigmoid(gate_pre)
    gate_act = gate_pre * sigmoid_gate
    hidden = (gate_act * up_pre).astype(jnp.bfloat16)
    d_hidden = jnp.dot(grad_rows, w_down, preferred_element_type=jnp.float32)
    d_gate = (d_hidden * up_pre * sigmoid_gate * (1.0 + gate_pre * (1.0 - sigmoid_gate))).astype(
        jnp.bfloat16
    )
    d_up = (d_hidden * gate_act).astype(jnp.bfloat16)
    mixed = jnp.concatenate([d_gate, d_up, hidden], axis=1)
    mixed_peer = lax.ppermute(mixed, "dp", across)
    mixed_all = jnp.concatenate([mixed, mixed_peer], axis=0)
    tok_all = jnp.concatenate([tok_mine, tok_peer], axis=0)
    grad_all = jnp.concatenate([grad_mine, grad_peer], axis=0)
    def late(d_gate, d_up):
        return (contract_cols(d_gate, w_gate) + contract_cols(d_up, w_up)).astype(jnp.bfloat16)

    summed, grad_tok = reduce_over_y(
        tok_all, grad_all, mixed_all, hidden.shape[1], late, (d_gate, d_up)
    )
    return (grad_tok, summed)


def reduce_over_y(tok_all, grad_all, mixed_all, cols, late, late_args):
    n = lax.axis_size("dp")
    nx = 2
    ny = n // nx
    y = lax.axis_index("dp") % ny
    rows, width = tok_all.shape
    lane = width // ny // 2
    tok_view = tok_all.reshape(rows, ny, 2 * lane)
    grad_view = grad_all.reshape(rows, ny, 2 * lane)
    d_both = mixed_all[:, : 2 * cols]
    hidden = mixed_all[:, 2 * cols :]

    def part_f(c):
        tok_part = lax.dynamic_index_in_dim(tok_view, c, axis=1, keepdims=False)
        return contract_rows(d_both, tok_part)

    def part_b(c):
        grad_part = lax.dynamic_index_in_dim(grad_view, c, axis=1, keepdims=False)
        return contract_rows(hidden, grad_part)

    fwd = [(a * ny + b, a * ny + (b + 1) % ny) for a in range(nx) for b in range(ny)]
    bwd = [(a * ny + b, a * ny + (b - 1) % ny) for a in range(nx) for b in range(ny)]
    acc_f = part_f((y + ny - 1) % ny)
    acc_b = part_b((y + 1) % ny)
    for s in range(ny - 1):
        recv_f = lax.ppermute(acc_f.astype(jnp.bfloat16), "dp", fwd)
        recv_b = lax.ppermute(acc_b.astype(jnp.bfloat16), "dp", bwd)
        if s == 0:
            recv_f, recv_b, late_args = lax.optimization_barrier((recv_f, recv_b, late_args))
            late_out = late(*late_args)
        scale = 1.0 / n if s == ny - 2 else 1.0
        acc_f = (recv_f.astype(jnp.float32) + part_f((y + 2 * ny - 2 - s) % ny)) * scale
        acc_b = (recv_b.astype(jnp.float32) + part_b((y + 2 + s) % ny)) * scale
    total = jnp.concatenate([acc_f, acc_b], axis=0).reshape(3, cols, 2 * lane)
    return jnp.transpose(total, (0, 2, 1)), late_out


def shards(tokens, cotangent, gate_weight, up_weight, down_weight, counts, seg_ids, pair_side):
    weights = token_weights(counts, seg_ids, pair_side)
    upstream = (cotangent.astype(jnp.float32) * weights[..., None]).astype(jnp.bfloat16)
    width = tokens.shape[-1]
    tok_rows = tokens.reshape(-1, width)
    grad_rows = upstream.reshape(-1, width)
    moved_rows, moved_grads = shifted((tok_rows, grad_rows), "blk", 1)
    n = lax.axis_size("dp")
    nb = lax.axis_size("blk")
    ny = n // 2
    xh = lax.axis_index("dp") // ny
    halves = (tok_rows.reshape(tok_rows.shape[0], 2, -1), grad_rows.reshape(grad_rows.shape[0], 2, -1))
    other = tuple(lax.dynamic_index_in_dim(h, 1 - xh, axis=1, keepdims=False) for h in halves)
    diagonal = [
        (d * nb + j, ((d + ny) % n) * nb + (j + 1) % nb) for d in range(n) for j in range(nb)
    ]
    tok_peer, grad_peer = lax.ppermute(other, ("dp", "blk"), diagonal)
    grad_moved, panel_grads = backward_core(
        moved_rows, moved_grads, tok_peer, grad_peer, gate_weight, up_weight, down_weight
    )
    grad_tok = shifted(grad_moved, "blk", -1)
    return (grad_tok.reshape(tokens.shape), panel_grads)


def solution(mesh):
    placed = (
        P("dp", "blk", None, None),
        P("dp", "blk", None, None),
        P(None, "blk"),
        P(None, "blk"),
        P(None, "blk"),
        P("dp", "blk"),
        P("dp", "blk", None),
        P("dp", "blk", None),
    )
    return jax.shard_map(
        shards,
        mesh=mesh,
        in_specs=placed,
        out_specs=(P("dp", "blk", None, None), P(None, "dp", "blk")),
        check_vma=False,
    )
```

```python
import jax
import jax.numpy as jnp
from jax import lax
from jax.sharding import PartitionSpec as P

CAP = 128
SEQS = 4


def shifted(block, axis, distance):
    devices = range(lax.axis_size(axis))
    route = [((i - distance) % len(devices), i) for i in devices]
    return lax.ppermute(block, axis, route)


def token_weights(counts, seg_ids, pair_side):
    positions = jnp.arange(seg_ids.shape[-1], dtype=jnp.int32)
    valid_rows = positions[None, None, :] < counts[:, :, None]
    member = (seg_ids[..., None] == jnp.arange(SEQS, dtype=jnp.int32)) & valid_rows[..., None]
    member_f = member.astype(jnp.float32)
    length = jnp.sum(member_f, axis=2)
    half_span = jnp.float32(CAP) / jnp.float32(SEQS)
    seq_weight = (2.0 * pair_side.astype(jnp.float32) - 1.0) * half_span / (length + half_span)
    return jnp.sum(member_f * seq_weight[:, :, None, :], axis=3)


def contract_rows(left, right):
    return lax.dot_general(
        left, right, (((0,), (0,)), ((), ())), preferred_element_type=jnp.float32
    )


def contract_cols(left, right):
    return lax.dot_general(
        left, right, (((1,), (1,)), ((), ())), preferred_element_type=jnp.float32
    )


def backward_core(tok_rows, grad_rows, tok_peer, grad_peer, w_gate, w_up, w_down):
    n = lax.axis_size("dp")
    nx = 2
    ny = n // nx
    xh = lax.axis_index("dp") // ny
    across = [(a * ny + b, (1 - a) * ny + b) for a in range(nx) for b in range(ny)]
    rows, width = tok_rows.shape
    tok_halves = tok_rows.reshape(rows, nx, width // nx)
    grad_halves = grad_rows.reshape(rows, nx, width // nx)
    tok_mine = lax.dynamic_index_in_dim(tok_halves, xh, axis=1, keepdims=False)
    grad_mine = lax.dynamic_index_in_dim(grad_halves, xh, axis=1, keepdims=False)

    gate_pre = jnp.dot(tok_rows, w_gate, preferred_element_type=jnp.float32)
    up_pre = jnp.dot(tok_rows, w_up, preferred_element_type=jnp.float32)
    sigmoid_gate = jax.nn.sigmoid(gate_pre)
    gate_act = gate_pre * sigmoid_gate
    hidden = (gate_act * up_pre).astype(jnp.bfloat16)
    d_hidden = jnp.dot(grad_rows, w_down, preferred_element_type=jnp.float32)
    d_gate = (d_hidden * up_pre * sigmoid_gate * (1.0 + gate_pre * (1.0 - sigmoid_gate))).astype(
        jnp.bfloat16
    )
    d_up = (d_hidden * gate_act).astype(jnp.bfloat16)
    mixed = jnp.concatenate([d_gate, d_up, hidden], axis=1)
    mixed_peer = lax.ppermute(mixed, "dp", across)
    mixed_all = jnp.concatenate([mixed, mixed_peer], axis=0)
    tok_all = jnp.concatenate([tok_mine, tok_peer], axis=0)
    grad_all = jnp.concatenate([grad_mine, grad_peer], axis=0)
    def late(d_gate, d_up):
        return (contract_cols(d_gate, w_gate) + contract_cols(d_up, w_up)).astype(jnp.bfloat16)

    summed, grad_tok = reduce_over_y(
        tok_all, grad_all, mixed_all, hidden.shape[1], late, (d_gate, d_up)
    )
    return (grad_tok, summed / n)


def reduce_over_y(tok_all, grad_all, mixed_all, cols, late, late_args):
    n = lax.axis_size("dp")
    nx = 2
    ny = n // nx
    y = lax.axis_index("dp") % ny
    rows, width = tok_all.shape
    lane = width // ny // 2
    tok_view = tok_all.reshape(rows, ny * 2, lane)
    grad_view = grad_all.reshape(rows, ny * 2, lane)
    d_both = mixed_all[:, : 2 * cols]
    hidden = mixed_all[:, 2 * cols :]

    def chunk(c, h):
        b = c * 2 + h
        tok_part = lax.dynamic_index_in_dim(tok_view, b, axis=1, keepdims=False)
        grad_part = lax.dynamic_index_in_dim(grad_view, b, axis=1, keepdims=False)
        first = contract_rows(d_both, tok_part)
        second = contract_rows(hidden, grad_part)
        return jnp.concatenate([first, second], axis=0)

    fwd = [(a * ny + b, a * ny + (b + 1) % ny) for a in range(nx) for b in range(ny)]
    bwd = [(a * ny + b, a * ny + (b - 1) % ny) for a in range(nx) for b in range(ny)]
    acc_f = chunk((y + ny - 1) % ny, 0)
    acc_b = chunk((y + 1) % ny, 1)
    for s in range(ny - 1):
        recv_f = lax.ppermute(acc_f.astype(jnp.bfloat16), "dp", fwd)
        recv_b = lax.ppermute(acc_b.astype(jnp.bfloat16), "dp", bwd)
        if s == 0:
            recv_f, recv_b, late_args = lax.optimization_barrier((recv_f, recv_b, late_args))
            late_out = late(*late_args)
        acc_f = recv_f.astype(jnp.float32) + chunk((y + 2 * ny - 2 - s) % ny, 0)
        acc_b = recv_b.astype(jnp.float32) + chunk((y + 2 + s) % ny, 1)
    total = jnp.concatenate([acc_f, acc_b], axis=1).reshape(3, cols, 2 * lane)
    return jnp.transpose(total, (0, 2, 1)), late_out


def shards(tokens, cotangent, gate_weight, up_weight, down_weight, counts, seg_ids, pair_side):
    weights = token_weights(counts, seg_ids, pair_side)
    width = tokens.shape[-1]
    tok_rows = tokens.reshape(-1, width)
    grad_rows = cotangent.reshape(-1, width)
    scale_rows = weights.reshape(-1, 1)
    moved_rows, moved_cot, moved_scale = shifted((tok_rows, grad_rows, scale_rows), "blk", 1)
    moved_grads = (moved_cot.astype(jnp.float32) * moved_scale).astype(jnp.bfloat16)
    n = lax.axis_size("dp")
    nb = lax.axis_size("blk")
    ny = n // 2
    xh = lax.axis_index("dp") // ny
    halves = (tok_rows.reshape(tok_rows.shape[0], 2, -1), grad_rows.reshape(grad_rows.shape[0], 2, -1))
    other = tuple(lax.dynamic_index_in_dim(h, 1 - xh, axis=1, keepdims=False) for h in halves)
    diagonal = [
        (d * nb + j, ((d + ny) % n) * nb + (j + 1) % nb) for d in range(n) for j in range(nb)
    ]
    tok_peer, cot_peer, scale_peer = lax.ppermute(other + (scale_rows,), ("dp", "blk"), diagonal)
    grad_peer = (cot_peer.astype(jnp.float32) * scale_peer).astype(jnp.bfloat16)
    grad_moved, panel_grads = backward_core(
        moved_rows, moved_grads, tok_peer, grad_peer, gate_weight, up_weight, down_weight
    )
    grad_tok = shifted(grad_moved, "blk", -1)
    return (grad_tok.reshape(tokens.shape), panel_grads)


def solution(mesh):
    placed = (
        P("dp", "blk", None, None),
        P("dp", "blk", None, None),
        P(None, "blk"),
        P(None, "blk"),
        P(None, "blk"),
        P("dp", "blk"),
        P("dp", "blk", None),
        P("dp", "blk", None),
    )
    return jax.shard_map(
        shards,
        mesh=mesh,
        in_specs=placed,
        out_specs=(P("dp", "blk", None, None), P(None, "dp", "blk")),
        check_vma=False,
    )
```
